256 devices in a mesh: row: 8 (over x, core), pair: 32 (over y, z).
Axes of the slice: x: 4, y: 4, z: 8, core: 2. Of those that a mesh axis runs over, the one named last changes fastest.
Arguments:
- weight: float32 [28672, 8192], P('row', 'pair'), may hold values from -300 to 300
- move_flags: int32 [2, 32], P(None, 'pair'), may hold values from 0 to 1
Outputs:
- columns: float32 [28672, 8192], P('row', 'pair')
- norm_ratios: float32 [8192], P('pair')
The draws below stay inside these ranges and needn't reach their ends.
All inputs are finite; a program needn't handle non-finite values.
Results may differ from the reference program's by a relative error of at most 0.0003.
Values sent between devices are 32-bit elements; how exact they have to be, the bound alone decides.
No kernel may reach another device: no remote copies, remote signals or barrier semaphores. Data moves between devices by JAX's collectives and lax.ppermute only.
A program may use at most 64 MiB of HBM per device.

```python
import math
import jax
import jax.numpy as jnp
from jax import lax

BLOCK = 128
SWEEPS = 2
POLAR = 8
ROUNDS = 3
M = 28672
N = 8192
N_PAIR = 32


def draw_weight(key, part):
    key_entries = jax.random.fold_in(key, 11)
    key_columns = jax.random.fold_in(key, 23)
    key_rows = jax.random.fold_in(key, 37)
    position = jnp.arange(N, dtype=jnp.float32) / (N - 1)
    col_scale = jnp.exp(position * math.log(3.0) + jax.random.uniform(key_columns, (N,), jnp.float32, 0.0, math.log(2.0)))
    entries = jax.random.truncated_normal(key_entries, -5.0, 5.0, (M, N), jnp.float32)
    row_scale = jnp.exp(jax.random.uniform(key_rows, (M,), jnp.float32, 0.0, math.log(10.0)))
    return entries * row_scale[:, None] * col_scale[None, :]


def set_ends(result, own_key, smallest, high):
    shape = result.shape
    place = [jax.random.randint(jax.random.fold_in(own_key, axis), (), 0, shape[axis]) for axis in range(len(shape))]
    result = result.at[tuple(place)].set(smallest)
    longest = shape.index(max(shape))
    place[longest] = (place[longest] + 1) % shape[longest]
    return result.at[tuple(place)].set(high)


def setup_inputs(seed: int = 0) -> dict:
    streams_of = jax.random.split(jax.random.key(seed), 3)
    weight = draw_weight(jax.random.fold_in(streams_of[2], 71), 0)
    move_flags = set_ends(jax.random.randint(streams_of[1], (ROUNDS - 1, N_PAIR), 0, 2), jax.random.fold_in(streams_of[1], 1), 0, 1).astype(jnp.int32)
    return {"weight": weight, "move_flags": move_flags}


precise = lax.Precision.HIGHEST

def contract(left, right):
    return lax.dot_general(left, right, (((0,), (0,)), ((), ())), precision=precise, preferred_element_type=jnp.float32)

def orthogonal_iteration(gram_pair):
    rotation = jnp.eye(gram_pair.shape[0], dtype=jnp.float32)
    for sweep_index in range(SWEEPS):
        product = jnp.dot(gram_pair, rotation, precision=precise, preferred_element_type=jnp.float32)
        normal = contract(product, product)
        scaled = product / jnp.sqrt(jnp.sqrt(jnp.sum(normal * normal)))
        for polar_index in range(POLAR):
            inner = contract(scaled, scaled)
            scaled = 1.5 * scaled - 0.5 * jnp.dot(scaled, inner, precision=precise, preferred_element_type=jnp.float32)
        rotation = scaled
    return rotation

def rotate_slot(matrix):
    gram_pair = contract(matrix, matrix)
    return jnp.dot(matrix, orthogonal_iteration(gram_pair), precision=precise, preferred_element_type=jnp.float32)

def reference(weight, move_flags):
    slots = weight.reshape(M, N_PAIR, 2 * BLOCK).transpose(1, 0, 2)
    rotated = slots
    for round_index in range(ROUNDS):
        rotated = lax.map(rotate_slot, slots)
        if round_index + 1 < ROUNDS:
            first_half = rotated[:, :, :BLOCK]
            second_half = rotated[:, :, BLOCK:]
            lead_moves = (move_flags[round_index] == 1)[:, None, None]
            staying = jnp.where(lead_moves, second_half, first_half)
            moving = jnp.where(lead_moves, first_half, second_half)
            slots = jnp.concatenate([staying, jnp.roll(moving, 1, axis=0)], axis=2)
    final_layout = rotated.transpose(1, 0, 2).reshape(M, N)
    squares_total = jnp.sum(final_layout * final_layout)
    divisor = jnp.sqrt(squares_total / (M * N))
    columns = final_layout / divisor
    norm_ratios = jnp.sqrt(lax.optimization_barrier(jnp.sum(final_layout * final_layout, axis=0)) / M) / divisor
    return (columns, norm_ratios)
```

```python
import jax
import jax.numpy as jnp
from jax import lax
from jax.sharding import PartitionSpec as P

SWEEPS = 2
POLAR = 8
ROUNDS = 3


precise = lax.Precision.HIGHEST


def from_behind(block, axis, distance):
    devices = range(lax.axis_size(axis))
    route = [((i - distance) % len(devices), i) for i in devices]
    return lax.ppermute(block, axis, route)


def butterfly_sum(value, axis):
    size = lax.axis_size(axis)
    if size & (size - 1):
        return lax.psum(value, axis)
    step = 1
    while step < size:
        route = [(i, i ^ step) for i in range(size)]
        value = value + lax.ppermute(value, axis, route)
        step *= 2
    return value


def contract(left, right):
    return lax.dot_general(
        left, right, (((0,), (0,)), ((), ())), precision=precise, preferred_element_type=jnp.float32
    )


def orthogonal_iteration(gram_pair):
    rotation = jnp.eye(gram_pair.shape[0], dtype=jnp.float32)
    for sweep_index in range(SWEEPS):
        product = jnp.dot(
            gram_pair, rotation, precision=precise, preferred_element_type=jnp.float32
        )
        normal = contract(product, product)
        scaled = product / jnp.sqrt(jnp.sqrt(jnp.sum(normal * normal)))
        for polar_index in range(POLAR):
            inner = contract(scaled, scaled)
            scaled = 1.5 * scaled - 0.5 * jnp.dot(
                scaled, inner, precision=precise, preferred_element_type=jnp.float32
            )
        rotation = scaled
    return rotation


def on_device(weight, move_flags):
    half_width = weight.shape[1] // 2
    row_count = weight.shape[0] * lax.axis_size("row")
    cell_count = row_count * weight.shape[1] * lax.axis_size("pair")
    current = weight
    rotated = weight
    turned = None
    for round_index in range(ROUNDS):
        gram_pair = butterfly_sum(contract(current, current), "row")
        rotation = orthogonal_iteration(gram_pair)
        if round_index + 1 < ROUNDS:
            swapped = jnp.concatenate([rotation[:, half_width:], rotation[:, :half_width]], axis=1)
            rotation = jnp.where(move_flags[round_index, 0] == 1, swapped, rotation)
        rotated = jnp.dot(current, rotation, precision=precise, preferred_element_type=jnp.float32)
        if round_index + 1 < ROUNDS:
            staying = rotated[:, :half_width]
            arrived = from_behind(rotated[:, half_width:], "pair", 1)
            current = jnp.concatenate([staying, arrived], axis=1)
        else:
            turned = jnp.sum(
                rotation
                * jnp.dot(gram_pair, rotation, precision=precise, preferred_element_type=jnp.float32),
                axis=0,
            )
    squares_total = butterfly_sum(jnp.sum(turned), "pair")
    divisor = jnp.sqrt(squares_total / cell_count)
    columns = rotated / divisor
    norm_ratios = jnp.sqrt(turned / row_count) / divisor
    return (columns, norm_ratios)


def solution(mesh):
    return jax.shard_map(
        on_device,
        mesh=mesh,
        in_specs=(P("row", "pair"), P(None, "pair")),
        out_specs=(P("row", "pair"), P("pair")),
        check_vma=False,
    )
```

```python
import jax
import jax.numpy as jnp
from jax import lax
from jax.sharding import PartitionSpec as P

SWEEPS = 2
POLAR = 8
ROUNDS = 3


precise = lax.Precision.HIGHEST


def from_behind(block, axis, distance):
    devices = range(lax.axis_size(axis))
    route = [((i - distance) % len(devices), i) for i in devices]
    return lax.ppermute(block, axis, route)


def butterfly_sum(value, axis):
    size = lax.axis_size(axis)
    if size & (size - 1):
        return lax.psum(value, axis)
    step = 1
    while step < size:
        route = [(i, i ^ step) for i in range(size)]
        value = value + lax.ppermute(value, axis, route)
        step *= 2
    return value


def contract(left, right):
    return lax.dot_general(
        left, right, (((0,), (0,)), ((), ())), precision=precise, preferred_element_type=jnp.float32
    )


def dot(left, right):
    return jnp.dot(left, right, precision=precise, preferred_element_type=jnp.float32)


def orthogonal_iteration(gram_pair):
    rotation = jnp.eye(gram_pair.shape[0], dtype=jnp.float32)
    for sweep_index in range(SWEEPS):
        product = dot(gram_pair, rotation)
        normal = contract(product, product)
        scaled = product / jnp.sqrt(jnp.sqrt(jnp.sum(normal * normal)))
        for polar_index in range(POLAR):
            inner = contract(scaled, scaled)
            scaled = 1.5 * scaled - 0.5 * dot(scaled, inner)
        rotation = scaled
    return rotation


def staying_first(rotation, flag):
    half_width = rotation.shape[1] // 2
    swapped = jnp.concatenate([rotation[:, half_width:], rotation[:, :half_width]], axis=1)
    return jnp.where(flag == 1, swapped, rotation)


def basis_of(current, flag):
    gram_pair = butterfly_sum(contract(current, current), "row")
    rotation = orthogonal_iteration(gram_pair)
    if flag is not None:
        rotation = staying_first(rotation, flag)
    return gram_pair, rotation


def on_device(weight, move_flags):
    assert ROUNDS == 3
    half_width = weight.shape[1] // 2
    row_count = weight.shape[0] * lax.axis_size("row")
    cell_count = row_count * weight.shape[1] * lax.axis_size("pair")

    previous = from_behind(weight, "pair", 1)
    _, basis = basis_of(weight, move_flags[0, 0])
    basis_behind = from_behind(basis, "pair", 1)
    rotated_behind = dot(previous, basis_behind)
    staying_behind = rotated_behind[:, :half_width]
    current = jnp.concatenate([dot(weight, basis[:, :half_width]), rotated_behind[:, half_width:]], axis=1)
    arrived_behind = from_behind(rotated_behind[:, half_width:], "pair", 1)

    _, basis = basis_of(current, move_flags[1, 0])
    basis_behind = from_behind(basis, "pair", 1)
    current_behind = jnp.concatenate([staying_behind, arrived_behind], axis=1)
    current = jnp.concatenate(
        [dot(current, basis[:, :half_width]), dot(current_behind, basis_behind[:, half_width:])], axis=1
    )

    gram_pair, rotation = basis_of(current, None)
    rotated = dot(current, rotation)
    turned = jnp.sum(rotation * dot(gram_pair, rotation), axis=0)
    rotated, turned = lax.optimization_barrier((rotated, turned))
    squares_total = butterfly_sum(jnp.sum(turned), "pair")
    divisor = jnp.sqrt(squares_total / cell_count)
    columns = rotated / divisor
    norm_ratios = jnp.sqrt(turned / row_count) / divisor
    return (columns, norm_ratios)


def solution(mesh):
    return jax.shard_map(
        on_device,
        mesh=mesh,
        in_specs=(P("row", "pair"), P(None, "pair")),
        out_specs=(P("row", "pair"), P("pair")),
        check_vma=False,
    )
```

```python
import jax
import jax.numpy as jnp
from jax import lax
from jax.sharding import PartitionSpec as P

SWEEPS = 2
POLAR = 8
ROUNDS = 3


precise = lax.Precision.HIGHEST


def from_behind(block, axis, distance):
    devices = range(lax.axis_size(axis))
    route = [((i - distance) % len(devices), i) for i in devices]
    return lax.ppermute(block, axis, route)


def butterfly_sum(value, axis):
    size = lax.axis_size(axis)
    if size & (size - 1):
        return lax.psum(value, axis)
    step = 1
    while step < size:
        route = [(i, i ^ step) for i in range(size)]
        value = value + lax.ppermute(value, axis, route)
        step *= 2
    return value


def contract(left, right):
    return lax.dot_general(
        left, right, (((0,), (0,)), ((), ())), precision=precise, preferred_element_type=jnp.float32
    )


def dot(left, right):
    return jnp.dot(left, right, precision=precise, preferred_element_type=jnp.float32)


def orthogonal_iteration(gram_pair):
    rotation = jnp.eye(gram_pair.shape[0], dtype=jnp.float32)
    for sweep_index in range(SWEEPS):
        product = dot(gram_pair, rotation)
        normal = contract(product, product)
        scaled = product / jnp.sqrt(jnp.sqrt(jnp.sum(normal * normal)))
        for polar_index in range(POLAR):
            inner = contract(scaled, scaled)
            scaled = 1.5 * scaled - 0.5 * dot(scaled, inner)
        rotation = scaled
    return rotation


def staying_first(rotation, flag):
    half_width = rotation.shape[1] // 2
    swapped = jnp.concatenate([rotation[:, half_width:], rotation[:, :half_width]], axis=1)
    return jnp.where(flag == 1, swapped, rotation)


def basis_of(current, flag):
    gram_pair = butterfly_sum(contract(current, current), "row")
    rotation = orthogonal_iteration(gram_pair)
    if flag is not None:
        rotation = staying_first(rotation, flag)
    return gram_pair, rotation


def on_device(weight, move_flags):
    assert ROUNDS == 3
    half_width = weight.shape[1] // 2
    row_count = weight.shape[0] * lax.axis_size("row")
    cell_count = row_count * weight.shape[1] * lax.axis_size("pair")

    split = weight.shape[0] // 2
    previous_top = from_behind(weight[:split], "pair", 1)
    _, basis = basis_of(weight, move_flags[0, 0])
    basis_behind = from_behind(basis, "pair", 1)
    rotated_own = dot(weight, basis)
    moving_bottom = from_behind(rotated_own[split:, half_width:], "pair", 1)
    staying_bottom = from_behind(rotated_own[split:, :half_width], "pair", 1)
    rotated_top = dot(previous_top, basis_behind)
    arrived = jnp.concatenate([rotated_top[:, half_width:], moving_bottom], axis=0)
    current = jnp.concatenate([rotated_own[:, :half_width], arrived], axis=1)
    staying_behind = jnp.concatenate([rotated_top[:, :half_width], staying_bottom], axis=0)
    arrived_behind = from_behind(arrived, "pair", 1)

    _, basis = basis_of(current, move_flags[1, 0])
    basis_behind = from_behind(basis, "pair", 1)
    current_behind = jnp.concatenate([staying_behind, arrived_behind], axis=1)
    current = jnp.concatenate(
        [dot(current, basis[:, :half_width]), dot(current_behind, basis_behind[:, half_width:])], axis=1
    )

    gram_pair, rotation = basis_of(current, None)
    rotated = dot(current, rotation)
    turned = jnp.sum(rotation * dot(gram_pair, rotation), axis=0)
    rotated, turned = lax.optimization_barrier((rotated, turned))
    squares_total = butterfly_sum(jnp.sum(turned), "pair")
    divisor = jnp.sqrt(squares_total / cell_count)
    columns = rotated / divisor
    norm_ratios = jnp.sqrt(turned / row_count) / divisor
    return (columns, norm_ratios)


def solution(mesh):
    return jax.shard_map(
        on_device,
        mesh=mesh,
        in_specs=(P("row", "pair"), P(None, "pair")),
        out_specs=(P("row", "pair"), P("pair")),
        check_vma=False,
    )
```

```python
import jax
import jax.numpy as jnp
from jax import lax
from jax.sharding import PartitionSpec as P
from jax.experimental import pallas as pl
from jax.experimental.pallas import tpu as pltpu

SWEEPS = 2
POLAR = 8
ROUNDS = 3


precise = lax.Precision.HIGHEST


def from_behind(block, axis, distance):
    devices = range(lax.axis_size(axis))
    route = [((i - distance) % len(devices), i) for i in devices]
    return lax.ppermute(block, axis, route)


def butterfly_sum(value, axis):
    size = lax.axis_size(axis)
    if size & (size - 1):
        return lax.psum(value, axis)
    step = 1
    while step < size:
        route = [(i, i ^ step) for i in range(size)]
        value = value + lax.ppermute(value, axis, route)
        step *= 2
    return value


def contract(left, right):
    return lax.dot_general(
        left, right, (((0,), (0,)), ((), ())), precision=precise, preferred_element_type=jnp.float32
    )


def dot(left, right):
    return jnp.dot(left, right, precision=precise, preferred_element_type=jnp.float32)


def orthogonal_iteration(gram_pair):
    rotation = jnp.eye(gram_pair.shape[0], dtype=jnp.float32)
    for sweep_index in range(SWEEPS):
        product = dot(gram_pair, rotation)
        normal = contract(product, product)
        scaled = product / jnp.sqrt(jnp.sqrt(jnp.sum(normal * normal)))
        for polar_index in range(POLAR):
            inner = contract(scaled, scaled)
            scaled = 1.5 * scaled - 0.5 * dot(scaled, inner)
        rotation = scaled
    return rotation


def eigen_kernel(gram_ref, basis_ref):
    gram_pair = gram_ref[...]
    rotation = None
    for sweep_index in range(SWEEPS):
        product = gram_pair if rotation is None else dot(gram_pair, rotation)
        normal = dot(product.T, product)
        total = jnp.sum(jnp.sum(normal * normal, axis=1, keepdims=True), axis=0, keepdims=True)
        scaled = product / jnp.sqrt(jnp.sqrt(total))
        for polar_index in range(POLAR):
            inner = dot(scaled.T, scaled)
            scaled = 1.5 * scaled - 0.5 * dot(scaled, inner)
        rotation = scaled
    basis_ref[...] = rotation


def orthogonal_iteration_kernel(gram_pair):
    return pl.pallas_call(
        eigen_kernel,
        out_shape=jax.ShapeDtypeStruct(gram_pair.shape, jnp.float32),
        in_specs=[pl.BlockSpec(memory_space=pltpu.VMEM)],
        out_specs=pl.BlockSpec(memory_space=pltpu.VMEM),
    )(gram_pair)


def staying_first(rotation, flag):
    half_width = rotation.shape[1] // 2
    swapped = jnp.concatenate([rotation[:, half_width:], rotation[:, :half_width]], axis=1)
    return jnp.where(flag == 1, swapped, rotation)


def basis_of(current, flag):
    gram_pair = butterfly_sum(contract(current, current), "row")
    rotation = orthogonal_iteration_kernel(gram_pair)
    if flag is not None:
        rotation = staying_first(rotation, flag)
    return gram_pair, rotation


def on_device(weight, move_flags):
    assert ROUNDS == 3
    half_width = weight.shape[1] // 2
    row_count = weight.shape[0] * lax.axis_size("row")
    cell_count = row_count * weight.shape[1] * lax.axis_size("pair")

    split = weight.shape[0] // 2
    previous_top = from_behind(weight[:split], "pair", 1)
    _, basis = basis_of(weight, move_flags[0, 0])
    basis_behind = from_behind(basis, "pair", 1)
    rotated_own = dot(weight, basis)
    moving_bottom = from_behind(rotated_own[split:, half_width:], "pair", 1)
    staying_bottom = from_behind(rotated_own[split:, :half_width], "pair", 1)
    rotated_top = dot(previous_top, basis_behind)
    arrived = jnp.concatenate([rotated_top[:, half_width:], moving_bottom], axis=0)
    current = jnp.concatenate([rotated_own[:, :half_width], arrived], axis=1)
    staying_behind = jnp.concatenate([rotated_top[:, :half_width], staying_bottom], axis=0)
    arrived_behind = from_behind(arrived, "pair", 1)

    _, basis = basis_of(current, move_flags[1, 0])
    basis_behind = from_behind(basis, "pair", 1)
    current_behind = jnp.concatenate([staying_behind, arrived_behind], axis=1)
    current = jnp.concatenate(
        [dot(current, basis[:, :half_width]), dot(current_behind, basis_behind[:, half_width:])], axis=1
    )

    gram_pair, rotation = basis_of(current, None)
    rotated = dot(current, rotation)
    turned = jnp.sum(rotation * dot(gram_pair, rotation), axis=0)
    rotated, turned = lax.optimization_barrier((rotated, turned))
    squares_total = butterfly_sum(jnp.sum(turned), "pair")
    divisor = jnp.sqrt(squares_total / cell_count)
    columns = rotated / divisor
    norm_ratios = jnp.sqrt(turned / row_count) / divisor
    return (columns, norm_ratios)


def solution(mesh):
    return jax.shard_map(
        on_device,
        mesh=mesh,
        in_specs=(P("row", "pair"), P(None, "pair")),
        out_specs=(P("row", "pair"), P("pair")),
        check_vma=False,
    )
```

```python
import jax
import jax.numpy as jnp
from jax import lax
from jax.sharding import PartitionSpec as P
from jax.experimental import pallas as pl
from jax.experimental.pallas import tpu as pltpu

SWEEPS = 2
POLAR = 8
ROUNDS = 3


precise = lax.Precision.HIGHEST


def from_behind(block, axis, distance):
    devices = range(lax.axis_size(axis))
    route = [((i - distance) % len(devices), i) for i in devices]
    return lax.ppermute(block, axis, route)


def butterfly_sum(value, axis):
    size = lax.axis_size(axis)
    if size & (size - 1):
        return lax.psum(value, axis)
    step = 1
    while step < size:
        route = [(i, i ^ step) for i in range(size)]
        value = value + lax.ppermute(value, axis, route)
        step *= 2
    return value


def contract(left, right):
    return lax.dot_general(
        left, right, (((0,), (0,)), ((), ())), precision=precise, preferred_element_type=jnp.float32
    )


def dot(left, right):
    return jnp.dot(left, right, precision=precise, preferred_element_type=jnp.float32)


def orthogonal_iteration(gram_pair):
    rotation = jnp.eye(gram_pair.shape[0], dtype=jnp.float32)
    for sweep_index in range(SWEEPS):
        product = dot(gram_pair, rotation)
        normal = contract(product, product)
        scaled = product / jnp.sqrt(jnp.sqrt(jnp.sum(normal * normal)))
        for polar_index in range(POLAR):
            inner = contract(scaled, scaled)
            scaled = 1.5 * scaled - 0.5 * dot(scaled, inner)
        rotation = scaled
    return rotation


def split_bf16(value):
    high = value.astype(jnp.bfloat16)
    low = (value - high.astype(jnp.float32)).astype(jnp.bfloat16)
    return high, low


def dot_split(left, right):
    left_high, left_low = left
    right_high, right_low = right
    def one(a, b):
        return jnp.dot(a, b, preferred_element_type=jnp.float32)
    return one(left_high, right_high) + (one(left_high, right_low) + one(left_low, right_high))


def eigen_kernel(gram_ref, basis_ref):
    gram_pair = gram_ref[...]
    gram_parts = split_bf16(gram_pair)
    rotation = None
    for sweep_index in range(SWEEPS):
        product = gram_pair if rotation is None else dot_split(gram_parts, split_bf16(rotation))
        normal = dot_split(split_bf16(product.T), split_bf16(product))
        total = jnp.sum(jnp.sum(normal * normal, axis=1, keepdims=True), axis=0, keepdims=True)
        scaled = product / jnp.sqrt(jnp.sqrt(total))
        for polar_index in range(POLAR):
            parts = split_bf16(scaled)
            inner = dot_split(split_bf16(scaled.T), parts)
            scaled = 1.5 * scaled - 0.5 * dot_split(parts, split_bf16(inner))
        rotation = scaled
    basis_ref[...] = rotation


def orthogonal_iteration_kernel(gram_pair):
    return pl.pallas_call(
        eigen_kernel,
        out_shape=jax.ShapeDtypeStruct(gram_pair.shape, jnp.float32),
        in_specs=[pl.BlockSpec(memory_space=pltpu.VMEM)],
        out_specs=pl.BlockSpec(memory_space=pltpu.VMEM),
    )(gram_pair)


def staying_first(rotation, flag):
    half_width = rotation.shape[1] // 2
    swapped = jnp.concatenate([rotation[:, half_width:], rotation[:, :half_width]], axis=1)
    return jnp.where(flag == 1, swapped, rotation)


def basis_of(current, flag):
    gram_pair = butterfly_sum(contract(current, current), "row")
    rotation = orthogonal_iteration_kernel(gram_pair)
    if flag is not None:
        rotation = staying_first(rotation, flag)
    return gram_pair, rotation


def on_device(weight, move_flags):
    assert ROUNDS == 3
    half_width = weight.shape[1] // 2
    row_count = weight.shape[0] * lax.axis_size("row")
    cell_count = row_count * weight.shape[1] * lax.axis_size("pair")

    split = weight.shape[0] // 2
    previous_top = from_behind(weight[:split], "pair", 1)
    _, basis = basis_of(weight, move_flags[0, 0])
    basis_behind = from_behind(basis, "pair", 1)
    rotated_own = dot(weight, basis)
    moving_bottom = from_behind(rotated_own[split:, half_width:], "pair", 1)
    staying_bottom = from_behind(rotated_own[split:, :half_width], "pair", 1)
    rotated_top = dot(previous_top, basis_behind)
    arrived = jnp.concatenate([rotated_top[:, half_width:], moving_bottom], axis=0)
    current = jnp.concatenate([rotated_own[:, :half_width], arrived], axis=1)
    staying_behind = jnp.concatenate([rotated_top[:, :half_width], staying_bottom], axis=0)
    arrived_behind = from_behind(arrived, "pair", 1)

    _, basis = basis_of(current, move_flags[1, 0])
    basis_behind = from_behind(basis, "pair", 1)
    current_behind = jnp.concatenate([staying_behind, arrived_behind], axis=1)
    current = jnp.concatenate(
        [dot(current, basis[:, :half_width]), dot(current_behind, basis_behind[:, half_width:])], axis=1
    )

    gram_pair, rotation = basis_of(current, None)
    rotated = dot(current, rotation)
    turned = jnp.sum(rotation * dot(gram_pair, rotation), axis=0)
    rotated, turned = lax.optimization_barrier((rotated, turned))
    squares_total = butterfly_sum(jnp.sum(turned), "pair")
    divisor = jnp.sqrt(squares_total / cell_count)
    columns = rotated / divisor
    norm_ratios = jnp.sqrt(turned / row_count) / divisor
    return (columns, norm_ratios)


def solution(mesh):
    return jax.shard_map(
        on_device,
        mesh=mesh,
        in_specs=(P("row", "pair"), P(None, "pair")),
        out_specs=(P("row", "pair"), P("pair")),
        check_vma=False,
    )
```

```python
import jax
import jax.numpy as jnp
from jax import lax
from jax.sharding import PartitionSpec as P
from jax.experimental import pallas as pl
from jax.experimental.pallas import tpu as pltpu

SWEEPS = 2
POLAR = 8
ROUNDS = 3


precise = lax.Precision.HIGH


def from_behind(block, axis, distance):
    devices = range(lax.axis_size(axis))
    route = [((i - distance) % len(devices), i) for i in devices]
    return lax.ppermute(block, axis, route)


def butterfly_sum(value, axis):
    size = lax.axis_size(axis)
    if size & (size - 1):
        return lax.psum(value, axis)
    step = 1
    while step < size:
        route = [(i, i ^ step) for i in range(size)]
        value = value + lax.ppermute(value, axis, route)
        step *= 2
    return value


def contract(left, right):
    return lax.dot_general(
        left, right, (((0,), (0,)), ((), ())), precision=precise, preferred_element_type=jnp.float32
    )


def dot(left, right):
    return jnp.dot(left, right, precision=precise, preferred_element_type=jnp.float32)


def orthogonal_iteration(gram_pair):
    rotation = jnp.eye(gram_pair.shape[0], dtype=jnp.float32)
    for sweep_index in range(SWEEPS):
        product = dot(gram_pair, rotation)
        normal = contract(product, product)
        scaled = product / jnp.sqrt(jnp.sqrt(jnp.sum(normal * normal)))
        for polar_index in range(POLAR):
            inner = contract(scaled, scaled)
            scaled = 1.5 * scaled - 0.5 * dot(scaled, inner)
        rotation = scaled
    return rotation


def split_bf16(value):
    high = value.astype(jnp.bfloat16)
    low = (value - high.astype(jnp.float32)).astype(jnp.bfloat16)
    return high, low


def dot_split(left, right):
    left_high, left_low = left
    right_high, right_low = right
    def one(a, b):
        return jnp.dot(a, b, preferred_element_type=jnp.float32)
    return one(left_high, right_high) + (one(left_high, right_low) + one(left_low, right_high))


def eigen_kernel(gram_ref, basis_ref):
    gram_pair = gram_ref[...]
    gram_parts = split_bf16(gram_pair)
    rotation = None
    for sweep_index in range(SWEEPS):
        product = gram_pair if rotation is None else dot_split(gram_parts, split_bf16(rotation))
        normal = dot_split(split_bf16(product.T), split_bf16(product))
        total = jnp.sum(jnp.sum(normal * normal, axis=1, keepdims=True), axis=0, keepdims=True)
        scaled = product / jnp.sqrt(jnp.sqrt(total))
        for polar_index in range(POLAR):
            parts = split_bf16(scaled)
            inner = dot_split(split_bf16(scaled.T), parts)
            scaled = 1.5 * scaled - 0.5 * dot_split(parts, split_bf16(inner))
        rotation = scaled
    basis_ref[...] = rotation


def orthogonal_iteration_kernel(gram_pair):
    return pl.pallas_call(
        eigen_kernel,
        out_shape=jax.ShapeDtypeStruct(gram_pair.shape, jnp.float32),
        in_specs=[pl.BlockSpec(memory_space=pltpu.VMEM)],
        out_specs=pl.BlockSpec(memory_space=pltpu.VMEM),
    )(gram_pair)


def staying_first(rotation, flag):
    half_width = rotation.shape[1] // 2
    swapped = jnp.concatenate([rotation[:, half_width:], rotation[:, :half_width]], axis=1)
    return jnp.where(flag == 1, swapped, rotation)


def basis_of(current, flag):
    gram_pair = butterfly_sum(contract(current, current), "row")
    rotation = orthogonal_iteration_kernel(gram_pair)
    if flag is not None:
        rotation = staying_first(rotation, flag)
    return gram_pair, rotation


def on_device(weight, move_flags):
    assert ROUNDS == 3
    half_width = weight.shape[1] // 2
    row_count = weight.shape[0] * lax.axis_size("row")
    cell_count = row_count * weight.shape[1] * lax.axis_size("pair")

    split = weight.shape[0] // 2
    previous_top = from_behind(weight[:split], "pair", 1)
    _, basis = basis_of(weight, move_flags[0, 0])
    basis_behind = from_behind(basis, "pair", 1)
    rotated_own = dot(weight, basis)
    moving_bottom = from_behind(rotated_own[split:, half_width:], "pair", 1)
    staying_bottom = from_behind(rotated_own[split:, :half_width], "pair", 1)
    rotated_top = dot(previous_top, basis_behind)
    arrived = jnp.concatenate([rotated_top[:, half_width:], moving_bottom], axis=0)
    current = jnp.concatenate([rotated_own[:, :half_width], arrived], axis=1)
    staying_behind = jnp.concatenate([rotated_top[:, :half_width], staying_bottom], axis=0)
    arrived_behind = from_behind(arrived, "pair", 1)

    _, basis = basis_of(current, move_flags[1, 0])
    basis_behind = from_behind(basis, "pair", 1)
    current_behind = jnp.concatenate([staying_behind, arrived_behind], axis=1)
    current = jnp.concatenate(
        [dot(current, basis[:, :half_width]), dot(current_behind, basis_behind[:, half_width:])], axis=1
    )

    gram_pair, rotation = basis_of(current, None)
    rotated = dot(current, rotation)
    turned = jnp.sum(rotation * dot(gram_pair, rotation), axis=0)
    rotated = lax.optimization_barrier(rotated)
    squares_total = butterfly_sum(jnp.sum(turned), "pair")
    divisor = jnp.sqrt(squares_total / cell_count)
    columns = rotated / divisor
    norm_ratios = jnp.sqrt(turned / row_count) / divisor
    return (columns, norm_ratios)


def solution(mesh):
    return jax.shard_map(
        on_device,
        mesh=mesh,
        in_specs=(P("row", "pair"), P(None, "pair")),
        out_specs=(P("row", "pair"), P("pair")),
        check_vma=False,
    )
```

```python
import jax
import jax.numpy as jnp
from jax import lax
from jax.sharding import PartitionSpec as P
from jax.experimental import pallas as pl
from jax.experimental.pallas import tpu as pltpu

SWEEPS = 2
POLAR = 8
ROUNDS = 3


precise = lax.Precision.HIGH


def from_behind(block, axis, distance):
    devices = range(lax.axis_size(axis))
    route = [((i - distance) % len(devices), i) for i in devices]
    return lax.ppermute(block, axis, route)


def butterfly_sum(value, axis):
    size = lax.axis_size(axis)
    if size & (size - 1):
        return lax.psum(value, axis)
    step = 1
    while step < size:
        route = [(i, i ^ step) for i in range(size)]
        value = value + lax.ppermute(value, axis, route)
        step *= 2
    return value


def contract(left, right):
    return lax.dot_general(
        left, right, (((0,), (0,)), ((), ())), precision=precise, preferred_element_type=jnp.float32
    )


def dot(left, right):
    return jnp.dot(left, right, precision=precise, preferred_element_type=jnp.float32)


def orthogonal_iteration(gram_pair):
    rotation = jnp.eye(gram_pair.shape[0], dtype=jnp.float32)
    for sweep_index in range(SWEEPS):
        product = dot(gram_pair, rotation)
        normal = contract(product, product)
        scaled = product / jnp.sqrt(jnp.sqrt(jnp.sum(normal * normal)))
        for polar_index in range(POLAR):
            inner = contract(scaled, scaled)
            scaled = 1.5 * scaled - 0.5 * dot(scaled, inner)
        rotation = scaled
    return rotation


def split_bf16(value):
    high = value.astype(jnp.bfloat16)
    low = (value - high.astype(jnp.float32)).astype(jnp.bfloat16)
    return high, low


def dot_split(left, right):
    left_high, left_low = left
    right_high, right_low = right
    def one(a, b):
        return jnp.dot(a, b, preferred_element_type=jnp.float32)
    return one(left_high, right_high) + (one(left_high, right_low) + one(left_low, right_high))


def eigen_kernel(gram_ref, basis_ref):
    gram_pair = gram_ref[...]
    gram_parts = split_bf16(gram_pair)
    rotation = None
    for sweep_index in range(SWEEPS):
        product = gram_pair if rotation is None else dot_split(gram_parts, split_bf16(rotation))
        normal = dot_split(split_bf16(product.T), split_bf16(product))
        total = jnp.sum(jnp.sum(normal * normal, axis=1, keepdims=True), axis=0, keepdims=True)
        scaled = product / jnp.sqrt(jnp.sqrt(total))
        for polar_index in range(POLAR):
            parts = split_bf16(scaled)
            inner = dot_split(split_bf16(scaled.T), parts)
            scaled = 1.5 * scaled - 0.5 * dot_split(parts, split_bf16(inner))
        rotation = scaled
    basis_ref[...] = rotation


def orthogonal_iteration_kernel(gram_pair):
    return pl.pallas_call(
        eigen_kernel,
        out_shape=jax.ShapeDtypeStruct(gram_pair.shape, jnp.float32),
        in_specs=[pl.BlockSpec(memory_space=pltpu.VMEM)],
        out_specs=pl.BlockSpec(memory_space=pltpu.VMEM),
    )(gram_pair)


def staying_first(rotation, flag):
    half_width = rotation.shape[1] // 2
    swapped = jnp.concatenate([rotation[:, half_width:], rotation[:, :half_width]], axis=1)
    return jnp.where(flag == 1, swapped, rotation)


def basis_of(current, flag):
    gram_pair = butterfly_sum(contract(current, current), "row")
    rotation = orthogonal_iteration_kernel(gram_pair)
    if flag is not None:
        rotation = staying_first(rotation, flag)
    return gram_pair, rotation


def on_device(weight, move_flags):
    assert ROUNDS == 3
    half_width = weight.shape[1] // 2
    row_count = weight.shape[0] * lax.axis_size("row")
    cell_count = row_count * weight.shape[1] * lax.axis_size("pair")

    split = weight.shape[0] // 2
    previous_top = from_behind(weight[:split], "pair", 1)
    _, basis = basis_of(weight, move_flags[0, 0])
    basis_behind = from_behind(basis, "pair", 1)
    rotated_own = dot(weight, basis)
    moving_bottom = from_behind(rotated_own[split:, half_width:], "pair", 1)
    keep = weight.shape[0] * 3 // 4
    staying_bottom = from_behind(rotated_own[split:keep, :half_width], "pair", 1)
    rotated_top = dot(previous_top, basis_behind)
    arrived = jnp.concatenate([rotated_top[:, half_width:], moving_bottom], axis=0)
    current = jnp.concatenate([rotated_own[:, :half_width], arrived], axis=1)
    staying_behind = jnp.concatenate([rotated_top[:, :half_width], staying_bottom], axis=0)
    arrived_behind = from_behind(arrived[:keep], "pair", 1)

    _, basis = basis_of(current, move_flags[1, 0])
    basis_behind = from_behind(basis, "pair", 1)
    rotated_own = dot(current, basis)
    moving_tail = from_behind(rotated_own[keep:, half_width:], "pair", 1)
    current_behind = jnp.concatenate([staying_behind, arrived_behind], axis=1)
    moving_head = dot(current_behind, basis_behind[:, half_width:])
    current = jnp.concatenate(
        [rotated_own[:, :half_width], jnp.concatenate([moving_head, moving_tail], axis=0)], axis=1
    )

    gram_pair, rotation = basis_of(current, None)
    rotated = dot(current, rotation)
    turned = jnp.sum(rotation * dot(gram_pair, rotation), axis=0)
    rotated = lax.optimization_barrier(rotated)
    squares_total = butterfly_sum(jnp.sum(turned), "pair")
    divisor = jnp.sqrt(squares_total / cell_count)
    columns = rotated / divisor
    norm_ratios = jnp.sqrt(turned / row_count) / divisor
    return (columns, norm_ratios)


def solution(mesh):
    return jax.shard_map(
        on_device,
        mesh=mesh,
        in_specs=(P("row", "pair"), P(None, "pair")),
        out_specs=(P("row", "pair"), P("pair")),
        check_vma=False,
    )
```

```python
import jax
import jax.numpy as jnp
from jax import lax
from jax.sharding import PartitionSpec as P
from jax.experimental import pallas as pl
from jax.experimental.pallas import tpu as pltpu

SWEEPS = 2
POLAR = 8
ROUNDS = 3


precise = lax.Precision.HIGH


def from_behind(block, axis, distance):
    devices = range(lax.axis_size(axis))
    route = [((i - distance) % len(devices), i) for i in devices]
    return lax.ppermute(block, axis, route)


def butterfly_sum(value, axis):
    size = lax.axis_size(axis)
    if size & (size - 1):
        return lax.psum(value, axis)
    step = 1
    while step < size:
        route = [(i, i ^ step) for i in range(size)]
        value = value + lax.ppermute(value, axis, route)
        step *= 2
    return value


def contract(left, right):
    return lax.dot_general(
        left, right, (((0,), (0,)), ((), ())), precision=precise, preferred_element_type=jnp.float32
    )


def dot(left, right):
    return jnp.dot(left, right, precision=precise, preferred_element_type=jnp.float32)


def orthogonal_iteration(gram_pair):
    rotation = jnp.eye(gram_pair.shape[0], dtype=jnp.float32)
    for sweep_index in range(SWEEPS):
        product = dot(gram_pair, rotation)
        normal = contract(product, product)
        scaled = product / jnp.sqrt(jnp.sqrt(jnp.sum(normal * normal)))
        for polar_index in range(POLAR):
            inner = contract(scaled, scaled)
            scaled = 1.5 * scaled - 0.5 * dot(scaled, inner)
        rotation = scaled
    return rotation


def split_bf16(value):
    high = value.astype(jnp.bfloat16)
    low = (value - high.astype(jnp.float32)).astype(jnp.bfloat16)
    return high, low


def dot_split(left, right):
    left_high, left_low = left
    right_high, right_low = right
    def one(a, b):
        return jnp.dot(a, b, preferred_element_type=jnp.float32)
    return one(left_high, right_high) + (one(left_high, right_low) + one(left_low, right_high))


def eigen_kernel(gram_ref, basis_ref):
    gram_pair = gram_ref[...]
    gram_parts = split_bf16(gram_pair)
    rotation = None
    for sweep_index in range(SWEEPS):
        product = gram_pair if rotation is None else dot_split(gram_parts, split_bf16(rotation))
        normal = dot_split(split_bf16(product.T), split_bf16(product))
        total = jnp.sum(jnp.sum(normal * normal, axis=1, keepdims=True), axis=0, keepdims=True)
        scaled = product / jnp.sqrt(jnp.sqrt(total))
        for polar_index in range(POLAR):
            parts = split_bf16(scaled)
            inner = dot_split(split_bf16(scaled.T), parts)
            scaled = 1.5 * scaled - 0.5 * dot_split(parts, split_bf16(inner))
        rotation = scaled
    basis_ref[...] = rotation


def orthogonal_iteration_kernel(gram_pair):
    return pl.pallas_call(
        eigen_kernel,
        out_shape=jax.ShapeDtypeStruct(gram_pair.shape, jnp.float32),
        in_specs=[pl.BlockSpec(memory_space=pltpu.VMEM)],
        out_specs=pl.BlockSpec(memory_space=pltpu.VMEM),
    )(gram_pair)


def staying_first(rotation, flag):
    half_width = rotation.shape[1] // 2
    swapped = jnp.concatenate([rotation[:, half_width:], rotation[:, :half_width]], axis=1)
    return jnp.where(flag == 1, swapped, rotation)


def basis_of(current, flag):
    gram_pair = butterfly_sum(contract(current, current), "row")
    rotation = orthogonal_iteration_kernel(gram_pair)
    if flag is not None:
        rotation = staying_first(rotation, flag)
    return gram_pair, rotation


def on_device(weight, move_flags):
    assert ROUNDS == 3
    half_width = weight.shape[1] // 2
    row_count = weight.shape[0] * lax.axis_size("row")
    cell_count = row_count * weight.shape[1] * lax.axis_size("pair")

    split = weight.shape[0] // 2
    previous_top = from_behind(weight[:split], "pair", 1)
    _, basis = basis_of(weight, move_flags[0, 0])
    basis_behind = from_behind(basis, "pair", 1)
    rotated_own = dot(weight, basis)
    moving_bottom = from_behind(rotated_own[split:, half_width:], "pair", 1)
    keep = weight.shape[0] * 5 // 8
    staying_bottom = from_behind(rotated_own[split:keep, :half_width], "pair", 1)
    rotated_top = dot(previous_top, basis_behind)
    arrived = jnp.concatenate([rotated_top[:, half_width:], moving_bottom], axis=0)
    current = jnp.concatenate([rotated_own[:, :half_width], arrived], axis=1)
    staying_behind = jnp.concatenate([rotated_top[:, :half_width], staying_bottom], axis=0)
    arrived_behind = from_behind(arrived[:keep], "pair", 1)

    _, basis = basis_of(current, move_flags[1, 0])
    basis_behind = from_behind(basis, "pair", 1)
    rotated_own = dot(current, basis)
    moving_tail = from_behind(rotated_own[keep:, half_width:], "pair", 1)
    current_behind = jnp.concatenate([staying_behind, arrived_behind], axis=1)
    moving_head = dot(current_behind, basis_behind[:, half_width:])
    current = jnp.concatenate(
        [rotated_own[:, :half_width], jnp.concatenate([moving_head, moving_tail], axis=0)], axis=1
    )

    gram_pair, rotation = basis_of(current, None)
    rotated = dot(current, rotation)
    turned = jnp.sum(rotation * dot(gram_pair, rotation), axis=0)
    rotated = lax.optimization_barrier(rotated)
    squares_total = butterfly_sum(jnp.sum(turned), "pair")
    divisor = jnp.sqrt(squares_total / cell_count)
    columns = rotated / divisor
    norm_ratios = jnp.sqrt(turned / row_count) / divisor
    return (columns, norm_ratios)


def solution(mesh):
    return jax.shard_map(
        on_device,
        mesh=mesh,
        in_specs=(P("row", "pair"), P(None, "pair")),
        out_specs=(P("row", "pair"), P("pair")),
        check_vma=False,
    )
```

```python
import jax
import jax.numpy as jnp
from jax import lax
from jax.sharding import PartitionSpec as P
from jax.experimental import pallas as pl
from jax.experimental.pallas import tpu as pltpu

SWEEPS = 2
POLAR = 8
ROUNDS = 3


precise = lax.Precision.HIGH


def from_behind(block, axis, distance):
    devices = range(lax.axis_size(axis))
    route = [((i - distance) % len(devices), i) for i in devices]
    return lax.ppermute(block, axis, route)


def butterfly_sum(value, axis):
    size = lax.axis_size(axis)
    if size & (size - 1):
        return lax.psum(value, axis)
    step = 1
    while step < size:
        route = [(i, i ^ step) for i in range(size)]
        value = value + lax.ppermute(value, axis, route)
        step *= 2
    return value


def contract(left, right):
    return lax.dot_general(
        left, right, (((0,), (0,)), ((), ())), precision=precise, preferred_element_type=jnp.float32
    )


def dot(left, right):
    return jnp.dot(left, right, precision=precise, preferred_element_type=jnp.float32)


def orthogonal_iteration(gram_pair):
    rotation = jnp.eye(gram_pair.shape[0], dtype=jnp.float32)
    for sweep_index in range(SWEEPS):
        product = dot(gram_pair, rotation)
        normal = contract(product, product)
        scaled = product / jnp.sqrt(jnp.sqrt(jnp.sum(normal * normal)))
        for polar_index in range(POLAR):
            inner = contract(scaled, scaled)
            scaled = 1.5 * scaled - 0.5 * dot(scaled, inner)
        rotation = scaled
    return rotation


def split_bf16(value):
    high = value.astype(jnp.bfloat16)
    low = (value - high.astype(jnp.float32)).astype(jnp.bfloat16)
    return high, low


def dot_split(left, right):
    left_high, left_low = left
    right_high, right_low = right
    def one(a, b):
        return jnp.dot(a, b, preferred_element_type=jnp.float32)
    return one(left_high, right_high) + (one(left_high, right_low) + one(left_low, right_high))


def eigen_kernel(gram_ref, basis_ref):
    gram_pair = gram_ref[...]
    gram_parts = split_bf16(gram_pair)
    rotation = None
    for sweep_index in range(SWEEPS):
        product = gram_pair if rotation is None else dot_split(gram_parts, split_bf16(rotation))
        normal = dot_split(split_bf16(product.T), split_bf16(product))
        total = jnp.sum(jnp.sum(normal * normal, axis=1, keepdims=True), axis=0, keepdims=True)
        scaled = product / jnp.sqrt(jnp.sqrt(total))
        for polar_index in range(POLAR):
            parts = split_bf16(scaled)
            inner = dot_split(split_bf16(scaled.T), parts)
            scaled = 1.5 * scaled - 0.5 * dot_split(parts, split_bf16(inner))
        rotation = scaled
    basis_ref[...] = rotation


def orthogonal_iteration_kernel(gram_pair):
    return pl.pallas_call(
        eigen_kernel,
        out_shape=jax.ShapeDtypeStruct(gram_pair.shape, jnp.float32),
        in_specs=[pl.BlockSpec(memory_space=pltpu.VMEM)],
        out_specs=pl.BlockSpec(memory_space=pltpu.VMEM),
    )(gram_pair)


def staying_first(rotation, flag):
    half_width = rotation.shape[1] // 2
    swapped = jnp.concatenate([rotation[:, half_width:], rotation[:, :half_width]], axis=1)
    return jnp.where(flag == 1, swapped, rotation)


def basis_of(current, flag):
    gram_pair = butterfly_sum(contract(current, current), "row")
    rotation = orthogonal_iteration_kernel(gram_pair)
    if flag is not None:
        rotation = staying_first(rotation, flag)
    return gram_pair, rotation


def on_device(weight, move_flags):
    assert ROUNDS == 3
    half_width = weight.shape[1] // 2
    row_count = weight.shape[0] * lax.axis_size("row")
    cell_count = row_count * weight.shape[1] * lax.axis_size("pair")

    split = weight.shape[0] // 2
    previous_top = from_behind(weight[:split], "pair", 1)
    _, basis = basis_of(weight, move_flags[0, 0])
    basis_behind = from_behind(basis, "pair", 1)
    rotated_own = dot(weight, basis)
    moving_bottom = from_behind(rotated_own[split:, half_width:], "pair", 1)
    keep = weight.shape[0] * 3 // 4
    staying_bottom = from_behind(rotated_own[split:keep, :half_width], "pair", 1)
    rotated_top = dot(previous_top, basis_behind)
    arrived = jnp.concatenate([rotated_top[:, half_width:], moving_bottom], axis=0)
    current = jnp.concatenate([rotated_own[:, :half_width], arrived], axis=1)
    staying_behind = jnp.concatenate([rotated_top[:, :half_width], staying_bottom], axis=0)
    arrived_behind = from_behind(arrived[:keep], "pair", 1)

    gram_pair, basis = basis_of(current, move_flags[1, 0])
    basis_behind = from_behind(basis, "pair", 1)
    gram_behind = from_behind(gram_pair, "pair", 1)
    rotated_own = dot(current, basis)
    moving_tail = from_behind(rotated_own[keep:, half_width:], "pair", 1)
    current_behind = jnp.concatenate([staying_behind, arrived_behind], axis=1)
    moving_head = dot(current_behind, basis_behind[:, half_width:])
    current = jnp.concatenate(
        [rotated_own[:, :half_width], jnp.concatenate([moving_head, moving_tail], axis=0)], axis=1
    )

    own_part = basis[:, :half_width]
    behind_part = basis_behind[:, half_width:]
    staying_gram = contract(own_part, dot(gram_pair, own_part))
    arriving_gram = contract(behind_part, dot(gram_behind, behind_part))
    cross = butterfly_sum(contract(current[:, :half_width], current[:, half_width:]), "row")
    gram_pair = jnp.concatenate(
        [
            jnp.concatenate([staying_gram, cross], axis=1),
            jnp.concatenate([cross.T, arriving_gram], axis=1),
        ],
        axis=0,
    )
    rotation = orthogonal_iteration_kernel(gram_pair)
    rotated = dot(current, rotation)
    turned = jnp.sum(rotation * dot(gram_pair, rotation), axis=0)
    rotated = lax.optimization_barrier(rotated)
    squares_total = butterfly_sum(jnp.sum(turned), "pair")
    divisor = jnp.sqrt(squares_total / cell_count)
    columns = rotated / divisor
    norm_ratios = jnp.sqrt(turned / row_count) / divisor
    return (columns, norm_ratios)


def solution(mesh):
    return jax.shard_map(
        on_device,
        mesh=mesh,
        in_specs=(P("row", "pair"), P(None, "pair")),
        out_specs=(P("row", "pair"), P("pair")),
        check_vma=False,
    )
```

```python
import jax
import jax.numpy as jnp
from jax import lax
from jax.sharding import PartitionSpec as P
from jax.experimental import pallas as pl
from jax.experimental.pallas import tpu as pltpu

SWEEPS = 2
POLAR = 8
ROUNDS = 3


precise = lax.Precision.HIGH


def from_behind(block, axis, distance):
    devices = range(lax.axis_size(axis))
    route = [((i - distance) % len(devices), i) for i in devices]
    return lax.ppermute(block, axis, route)


def butterfly_sum(value, axis):
    size = lax.axis_size(axis)
    if size & (size - 1):
        return lax.psum(value, axis)
    step = 1
    while step < size:
        route = [(i, i ^ step) for i in range(size)]
        value = value + lax.ppermute(value, axis, route)
        step *= 2
    return value


def contract(left, right):
    return lax.dot_general(
        left, right, (((0,), (0,)), ((), ())), precision=precise, preferred_element_type=jnp.float32
    )


def dot(left, right):
    return jnp.dot(left, right, precision=precise, preferred_element_type=jnp.float32)


def orthogonal_iteration(gram_pair):
    rotation = jnp.eye(gram_pair.shape[0], dtype=jnp.float32)
    for sweep_index in range(SWEEPS):
        product = dot(gram_pair, rotation)
        normal = contract(product, product)
        scaled = product / jnp.sqrt(jnp.sqrt(jnp.sum(normal * normal)))
        for polar_index in range(POLAR):
            inner = contract(scaled, scaled)
            scaled = 1.5 * scaled - 0.5 * dot(scaled, inner)
        rotation = scaled
    return rotation


def split_bf16(value):
    high = value.astype(jnp.bfloat16)
    low = (value - high.astype(jnp.float32)).astype(jnp.bfloat16)
    return high, low


def dot_split(left, right):
    left_high, left_low = left
    right_high, right_low = right
    def one(a, b):
        return jnp.dot(a, b, preferred_element_type=jnp.float32)
    return one(left_high, right_high) + (one(left_high, right_low) + one(left_low, right_high))


def eigen_kernel(gram_ref, basis_ref):
    gram_pair = gram_ref[...]
    gram_parts = split_bf16(gram_pair)
    rotation = None
    for sweep_index in range(SWEEPS):
        product = gram_pair if rotation is None else dot_split(gram_parts, split_bf16(rotation))
        normal = dot_split(split_bf16(product.T), split_bf16(product))
        total = jnp.sum(jnp.sum(normal * normal, axis=1, keepdims=True), axis=0, keepdims=True)
        scaled = product / jnp.sqrt(jnp.sqrt(total))
        for polar_index in range(POLAR):
            parts = split_bf16(scaled)
            inner = dot_split(split_bf16(scaled.T), parts)
            scaled = 1.5 * scaled - 0.5 * dot_split(parts, split_bf16(inner))
        rotation = scaled
    basis_ref[...] = rotation


def orthogonal_iteration_kernel(gram_pair):
    return pl.pallas_call(
        eigen_kernel,
        out_shape=jax.ShapeDtypeStruct(gram_pair.shape, jnp.float32),
        in_specs=[pl.BlockSpec(memory_space=pltpu.VMEM)],
        out_specs=pl.BlockSpec(memory_space=pltpu.VMEM),
    )(gram_pair)


def staying_first(rotation, flag):
    half_width = rotation.shape[1] // 2
    swapped = jnp.concatenate([rotation[:, half_width:], rotation[:, :half_width]], axis=1)
    return jnp.where(flag == 1, swapped, rotation)


def basis_of(current, flag):
    gram_pair = butterfly_sum(contract(current, current), "row")
    rotation = orthogonal_iteration_kernel(gram_pair)
    if flag is not None:
        rotation = staying_first(rotation, flag)
    return gram_pair, rotation


def on_device(weight, move_flags):
    assert ROUNDS == 3
    half_width = weight.shape[1] // 2
    row_count = weight.shape[0] * lax.axis_size("row")
    cell_count = row_count * weight.shape[1] * lax.axis_size("pair")

    split = weight.shape[0] // 2
    previous_top = from_behind(weight[:split], "pair", 1)
    _, basis = basis_of(weight, move_flags[0, 0])
    basis_behind = from_behind(basis, "pair", 1)
    rotated_own = dot(weight, basis)
    moving_bottom = from_behind(rotated_own[split:, half_width:], "pair", 1)
    keep = weight.shape[0] * 3 // 4
    staying_bottom = from_behind(rotated_own[split:keep, :half_width], "pair", 1)
    rotated_top = dot(previous_top, basis_behind)
    arrived = jnp.concatenate([rotated_top[:, half_width:], moving_bottom], axis=0)
    current = jnp.concatenate([rotated_own[:, :half_width], arrived], axis=1)
    staying_behind = jnp.concatenate([rotated_top[:, :half_width], staying_bottom], axis=0)
    arrived_behind = from_behind(arrived[:keep], "pair", 1)

    gram_pair, basis = basis_of(current, move_flags[1, 0])
    basis_behind = from_behind(basis, "pair", 1)
    moving_part = basis[:, half_width:]
    arriving_gram = from_behind(contract(moving_part, dot(gram_pair, moving_part)), "pair", 1)
    rotated_own = dot(current, basis)
    moving_tail = from_behind(rotated_own[keep:, half_width:], "pair", 1)
    current_behind = jnp.concatenate([staying_behind, arrived_behind], axis=1)
    moving_head = dot(current_behind, basis_behind[:, half_width:])
    current = jnp.concatenate(
        [rotated_own[:, :half_width], jnp.concatenate([moving_head, moving_tail], axis=0)], axis=1
    )

    own_part = basis[:, :half_width]
    staying_gram = contract(own_part, dot(gram_pair, own_part))
    cross = butterfly_sum(contract(current[:, :half_width], current[:, half_width:]), "row")
    gram_pair = jnp.concatenate(
        [
            jnp.concatenate([staying_gram, cross], axis=1),
            jnp.concatenate([cross.T, arriving_gram], axis=1),
        ],
        axis=0,
    )
    rotation = orthogonal_iteration_kernel(gram_pair)
    rotated = dot(current, rotation)
    turned = jnp.sum(rotation * dot(gram_pair, rotation), axis=0)
    rotated = lax.optimization_barrier(rotated)
    squares_total = butterfly_sum(jnp.sum(turned), "pair")
    divisor = jnp.sqrt(squares_total / cell_count)
    columns = rotated / divisor
    norm_ratios = jnp.sqrt(turned / row_count) / divisor
    return (columns, norm_ratios)


def solution(mesh):
    return jax.shard_map(
        on_device,
        mesh=mesh,
        in_specs=(P("row", "pair"), P(None, "pair")),
        out_specs=(P("row", "pair"), P("pair")),
        check_vma=False,
    )
```

```python
import jax
import jax.numpy as jnp
from jax import lax
from jax.sharding import PartitionSpec as P
from jax.experimental import pallas as pl
from jax.experimental.pallas import tpu as pltpu

SWEEPS = 2
POLAR = 8
ROUNDS = 3


precise = lax.Precision.HIGH


def from_behind(block, axis, distance):
    devices = range(lax.axis_size(axis))
    route = [((i - distance) % len(devices), i) for i in devices]
    return lax.ppermute(block, axis, route)


def butterfly_sum(value, axis):
    size = lax.axis_size(axis)
    if size & (size - 1):
        return lax.psum(value, axis)
    step = 1
    while step < size:
        route = [(i, i ^ step) for i in range(size)]
        value = value + lax.ppermute(value, axis, route)
        step *= 2
    return value


def contract(left, right):
    return lax.dot_general(
        left, right, (((0,), (0,)), ((), ())), precision=precise, preferred_element_type=jnp.float32
    )


def dot(left, right):
    return jnp.dot(left, right, precision=precise, preferred_element_type=jnp.float32)


def orthogonal_iteration(gram_pair):
    rotation = jnp.eye(gram_pair.shape[0], dtype=jnp.float32)
    for sweep_index in range(SWEEPS):
        product = dot(gram_pair, rotation)
        normal = contract(product, product)
        scaled = product / jnp.sqrt(jnp.sqrt(jnp.sum(normal * normal)))
        for polar_index in range(POLAR):
            inner = contract(scaled, scaled)
            scaled = 1.5 * scaled - 0.5 * dot(scaled, inner)
        rotation = scaled
    return rotation


def split_bf16(value):
    high = value.astype(jnp.bfloat16)
    low = (value - high.astype(jnp.float32)).astype(jnp.bfloat16)
    return high, low


def dot_split(left, right):
    left_high, left_low = left
    right_high, right_low = right
    def one(a, b):
        return jnp.dot(a, b, preferred_element_type=jnp.float32)
    return one(left_high, right_high) + (one(left_high, right_low) + one(left_low, right_high))


def eigen_kernel(gram_ref, basis_ref):
    gram_pair = gram_ref[...]
    gram_parts = split_bf16(gram_pair)
    rotation = None
    for sweep_index in range(SWEEPS):
        product = gram_pair if rotation is None else dot_split(gram_parts, split_bf16(rotation))
        normal = dot_split(split_bf16(product.T), split_bf16(product))
        total = jnp.sum(jnp.sum(normal * normal, axis=1, keepdims=True), axis=0, keepdims=True)
        scaled = product / jnp.sqrt(jnp.sqrt(total))
        for polar_index in range(POLAR):
            parts = split_bf16(scaled)
            inner = dot_split(split_bf16(scaled.T), parts)
            scaled = 1.5 * scaled - 0.5 * dot_split(parts, split_bf16(inner))
        rotation = scaled
    basis_ref[...] = rotation


def orthogonal_iteration_kernel(gram_pair):
    return pl.pallas_call(
        eigen_kernel,
        out_shape=jax.ShapeDtypeStruct(gram_pair.shape, jnp.float32),
        in_specs=[pl.BlockSpec(memory_space=pltpu.VMEM)],
        out_specs=pl.BlockSpec(memory_space=pltpu.VMEM),
    )(gram_pair)


def staying_first(rotation, flag):
    half_width = rotation.shape[1] // 2
    swapped = jnp.concatenate([rotation[:, half_width:], rotation[:, :half_width]], axis=1)
    return jnp.where(flag == 1, swapped, rotation)


def basis_of(current, flag):
    gram_pair = butterfly_sum(contract(current, current), "row")
    rotation = orthogonal_iteration_kernel(gram_pair)
    if flag is not None:
        rotation = staying_first(rotation, flag)
    return gram_pair, rotation


def gram_from_blocks(current, last_gram, own_part, arriving_gram):
    half_width = current.shape[1] // 2
    staying_gram = contract(own_part, dot(last_gram, own_part))
    cross = butterfly_sum(contract(current[:, :half_width], current[:, half_width:]), "row")
    return jnp.concatenate(
        [
            jnp.concatenate([staying_gram, cross], axis=1),
            jnp.concatenate([cross.T, arriving_gram], axis=1),
        ],
        axis=0,
    )


def on_device(weight, move_flags):
    assert ROUNDS == 3
    half_width = weight.shape[1] // 2
    row_count = weight.shape[0] * lax.axis_size("row")
    cell_count = row_count * weight.shape[1] * lax.axis_size("pair")

    split = weight.shape[0] // 2
    previous_top = from_behind(weight[:split], "pair", 1)
    gram_pair, basis = basis_of(weight, move_flags[0, 0])
    basis_behind = from_behind(basis, "pair", 1)
    moving_part = basis[:, half_width:]
    arriving_gram = from_behind(contract(moving_part, dot(gram_pair, moving_part)), "pair", 1)
    rotated_own = dot(weight, basis)
    moving_bottom = from_behind(rotated_own[split:, half_width:], "pair", 1)
    keep = weight.shape[0] * 3 // 4
    staying_bottom = from_behind(rotated_own[split:keep, :half_width], "pair", 1)
    rotated_top = dot(previous_top, basis_behind)
    arrived = jnp.concatenate([rotated_top[:, half_width:], moving_bottom], axis=0)
    current = jnp.concatenate([rotated_own[:, :half_width], arrived], axis=1)
    staying_behind = jnp.concatenate([rotated_top[:, :half_width], staying_bottom], axis=0)
    arrived_behind = from_behind(arrived[:keep], "pair", 1)

    gram_pair = gram_from_blocks(current, gram_pair, basis[:, :half_width], arriving_gram)
    basis = staying_first(orthogonal_iteration_kernel(gram_pair), move_flags[1, 0])
    basis_behind = from_behind(basis, "pair", 1)
    moving_part = basis[:, half_width:]
    arriving_gram = from_behind(contract(moving_part, dot(gram_pair, moving_part)), "pair", 1)
    rotated_own = dot(current, basis)
    moving_tail = from_behind(rotated_own[keep:, half_width:], "pair", 1)
    current_behind = jnp.concatenate([staying_behind, arrived_behind], axis=1)
    moving_head = dot(current_behind, basis_behind[:, half_width:])
    current = jnp.concatenate(
        [rotated_own[:, :half_width], jnp.concatenate([moving_head, moving_tail], axis=0)], axis=1
    )

    gram_pair = gram_from_blocks(current, gram_pair, basis[:, :half_width], arriving_gram)
    rotation = orthogonal_iteration_kernel(gram_pair)
    rotated = dot(current, rotation)
    turned = jnp.sum(rotation * dot(gram_pair, rotation), axis=0)
    rotated = lax.optimization_barrier(rotated)
    squares_total = butterfly_sum(jnp.sum(turned), "pair")
    divisor = jnp.sqrt(squares_total / cell_count)
    columns = rotated / divisor
    norm_ratios = jnp.sqrt(turned / row_count) / divisor
    return (columns, norm_ratios)


def solution(mesh):
    return jax.shard_map(
        on_device,
        mesh=mesh,
        in_specs=(P("row", "pair"), P(None, "pair")),
        out_specs=(P("row", "pair"), P("pair")),
        check_vma=False,
    )
```

```python
import jax
import jax.numpy as jnp
from jax import lax
from jax.sharding import PartitionSpec as P
from jax.experimental import pallas as pl
from jax.experimental.pallas import tpu as pltpu

SWEEPS = 2
POLAR = 8
ROUNDS = 3


precise = lax.Precision.HIGH


def from_behind(block, axis, distance):
    devices = range(lax.axis_size(axis))
    route = [((i - distance) % len(devices), i) for i in devices]
    return lax.ppermute(block, axis, route)


def butterfly_sum(value, axis):
    size = lax.axis_size(axis)
    if size & (size - 1):
        return lax.psum(value, axis)
    step = 1
    while step < size:
        route = [(i, i ^ step) for i in range(size)]
        value = value + lax.ppermute(value, axis, route)
        step *= 2
    return value


def contract(left, right):
    return lax.dot_general(
        left, right, (((0,), (0,)), ((), ())), precision=precise, preferred_element_type=jnp.float32
    )


def dot(left, right):
    return jnp.dot(left, right, precision=precise, preferred_element_type=jnp.float32)


def orthogonal_iteration(gram_pair):
    rotation = jnp.eye(gram_pair.shape[0], dtype=jnp.float32)
    for sweep_index in range(SWEEPS):
        product = dot(gram_pair, rotation)
        normal = contract(product, product)
        scaled = product / jnp.sqrt(jnp.sqrt(jnp.sum(normal * normal)))
        for polar_index in range(POLAR):
            inner = contract(scaled, scaled)
            scaled = 1.5 * scaled - 0.5 * dot(scaled, inner)
        rotation = scaled
    return rotation


def split_bf16(value):
    high = value.astype(jnp.bfloat16)
    low = (value - high.astype(jnp.float32)).astype(jnp.bfloat16)
    return high, low


def dot_split(left, right):
    left_high, left_low = left
    right_high, right_low = right
    def one(a, b):
        return jnp.dot(a, b, preferred_element_type=jnp.float32)
    return one(left_high, right_high) + (one(left_high, right_low) + one(left_low, right_high))


def eigen_kernel(gram_ref, basis_ref):
    gram_pair = gram_ref[...]
    gram_parts = split_bf16(gram_pair)
    rotation = None
    for sweep_index in range(SWEEPS):
        product = gram_pair if rotation is None else dot_split(gram_parts, split_bf16(rotation))
        normal = dot_split(split_bf16(product.T), split_bf16(product))
        total = jnp.sum(jnp.sum(normal * normal, axis=1, keepdims=True), axis=0, keepdims=True)
        scaled = product / jnp.sqrt(jnp.sqrt(total))
        for polar_index in range(POLAR):
            parts = split_bf16(scaled)
            inner = dot_split(split_bf16(scaled.T), parts)
            scaled = 1.5 * scaled - 0.5 * dot_split(parts, split_bf16(inner))
        rotation = scaled
    basis_ref[...] = rotation


def orthogonal_iteration_kernel(gram_pair):
    return pl.pallas_call(
        eigen_kernel,
        out_shape=jax.ShapeDtypeStruct(gram_pair.shape, jnp.float32),
        in_specs=[pl.BlockSpec(memory_space=pltpu.VMEM)],
        out_specs=pl.BlockSpec(memory_space=pltpu.VMEM),
    )(gram_pair)


def staying_first(rotation, flag):
    half_width = rotation.shape[1] // 2
    swapped = jnp.concatenate([rotation[:, half_width:], rotation[:, :half_width]], axis=1)
    return jnp.where(flag == 1, swapped, rotation)


def basis_of(current, flag):
    gram_pair = butterfly_sum(contract(current, current), "row")
    rotation = orthogonal_iteration_kernel(gram_pair)
    if flag is not None:
        rotation = staying_first(rotation, flag)
    return gram_pair, rotation


def on_device(weight, move_flags):
    assert ROUNDS == 3
    half_width = weight.shape[1] // 2
    row_count = weight.shape[0] * lax.axis_size("row")
    cell_count = row_count * weight.shape[1] * lax.axis_size("pair")

    split = weight.shape[0] // 2
    previous_top = from_behind(weight[:split], "pair", 1)
    first_gram, basis = basis_of(weight, move_flags[0, 0])
    basis_behind = from_behind(basis, "pair", 1)
    rotated_own = dot(weight, basis)
    moving_bottom = from_behind(rotated_own[split:, half_width:], "pair", 1)
    keep = weight.shape[0] * 3 // 4
    staying_bottom = from_behind(rotated_own[split:keep, :half_width], "pair", 1)
    rotated_top = dot(previous_top, basis_behind)
    arrived = jnp.concatenate([rotated_top[:, half_width:], moving_bottom], axis=0)
    current = jnp.concatenate([rotated_own[:, :half_width], arrived], axis=1)
    staying_behind = jnp.concatenate([rotated_top[:, :half_width], staying_bottom], axis=0)
    arrived_behind = from_behind(arrived[:keep], "pair", 1)

    own_part = basis[:, :half_width]
    staying_gram = contract(own_part, dot(first_gram, own_part))
    with_arrived = butterfly_sum(contract(current, current[:, half_width:]), "row")
    gram_pair = jnp.concatenate(
        [
            jnp.concatenate([staying_gram, with_arrived[:half_width]], axis=1),
            jnp.concatenate([with_arrived[:half_width].T, with_arrived[half_width:]], axis=1),
        ],
        axis=0,
    )
    basis = staying_first(orthogonal_iteration_kernel(gram_pair), move_flags[1, 0])
    basis_behind = from_behind(basis, "pair", 1)
    moving_part = basis[:, half_width:]
    arriving_gram = from_behind(contract(moving_part, dot(gram_pair, moving_part)), "pair", 1)
    rotated_own = dot(current, basis)
    moving_tail = from_behind(rotated_own[keep:, half_width:], "pair", 1)
    current_behind = jnp.concatenate([staying_behind, arrived_behind], axis=1)
    moving_head = dot(current_behind, basis_behind[:, half_width:])
    current = jnp.concatenate(
        [rotated_own[:, :half_width], jnp.concatenate([moving_head, moving_tail], axis=0)], axis=1
    )

    own_part = basis[:, :half_width]
    staying_gram = contract(own_part, dot(gram_pair, own_part))
    cross = butterfly_sum(contract(current[:, :half_width], current[:, half_width:]), "row")
    gram_pair = jnp.concatenate(
        [
            jnp.concatenate([staying_gram, cross], axis=1),
            jnp.concatenate([cross.T, arriving_gram], axis=1),
        ],
        axis=0,
    )
    rotation = orthogonal_iteration_kernel(gram_pair)
    rotated = dot(current, rotation)
    turned = jnp.sum(rotation * dot(gram_pair, rotation), axis=0)
    rotated = lax.optimization_barrier(rotated)
    squares_total = butterfly_sum(jnp.sum(turned), "pair")
    divisor = jnp.sqrt(squares_total / cell_count)
    columns = rotated / divisor
    norm_ratios = jnp.sqrt(turned / row_count) / divisor
    return (columns, norm_ratios)


def solution(mesh):
    return jax.shard_map(
        on_device,
        mesh=mesh,
        in_specs=(P("row", "pair"), P(None, "pair")),
        out_specs=(P("row", "pair"), P("pair")),
        check_vma=False,
    )
```

```python
import jax
import jax.numpy as jnp
from jax import lax
from jax.sharding import PartitionSpec as P
from jax.experimental import pallas as pl
from jax.experimental.pallas import tpu as pltpu

SWEEPS = 2
POLAR = 8
ROUNDS = 3


precise = lax.Precision.HIGH


def from_behind(block, axis, distance):
    devices = range(lax.axis_size(axis))
    route = [((i - distance) % len(devices), i) for i in devices]
    return lax.ppermute(block, axis, route)


def butterfly_sum(value, axis):
    size = lax.axis_size(axis)
    if size & (size - 1):
        return lax.psum(value, axis)
    step = 1
    while step < size:
        route = [(i, i ^ step) for i in range(size)]
        value = value + lax.ppermute(value, axis, route)
        step *= 2
    return value


def contract(left, right):
    return lax.dot_general(
        left, right, (((0,), (0,)), ((), ())), precision=precise, preferred_element_type=jnp.float32
    )


def dot(left, right):
    return jnp.dot(left, right, precision=precise, preferred_element_type=jnp.float32)


def orthogonal_iteration(gram_pair):
    rotation = jnp.eye(gram_pair.shape[0], dtype=jnp.float32)
    for sweep_index in range(SWEEPS):
        product = dot(gram_pair, rotation)
        normal = contract(product, product)
        scaled = product / jnp.sqrt(jnp.sqrt(jnp.sum(normal * normal)))
        for polar_index in range(POLAR):
            inner = contract(scaled, scaled)
            scaled = 1.5 * scaled - 0.5 * dot(scaled, inner)
        rotation = scaled
    return rotation


def split_bf16(value):
    high = value.astype(jnp.bfloat16)
    low = (value - high.astype(jnp.float32)).astype(jnp.bfloat16)
    return high, low


def dot_split(left, right):
    left_high, left_low = left
    right_high, right_low = right
    def one(a, b):
        return jnp.dot(a, b, preferred_element_type=jnp.float32)
    return one(left_high, right_high) + (one(left_high, right_low) + one(left_low, right_high))


def eigen_kernel(gram_ref, basis_ref):
    gram_pair = gram_ref[...]
    gram_parts = split_bf16(gram_pair)
    rotation = None
    for sweep_index in range(SWEEPS):
        product = gram_pair if rotation is None else dot_split(gram_parts, split_bf16(rotation))
        normal = dot_split(split_bf16(product.T), split_bf16(product))
        total = jnp.sum(jnp.sum(normal * normal, axis=1, keepdims=True), axis=0, keepdims=True)
        scaled = product / jnp.sqrt(jnp.sqrt(total))
        for polar_index in range(POLAR):
            parts = split_bf16(scaled)
            inner = dot_split(split_bf16(scaled.T), parts)
            scaled = 1.5 * scaled - 0.5 * dot_split(parts, split_bf16(inner))
        rotation = scaled
    basis_ref[...] = rotation


def orthogonal_iteration_kernel(gram_pair):
    return pl.pallas_call(
        eigen_kernel,
        out_shape=jax.ShapeDtypeStruct(gram_pair.shape, jnp.float32),
        in_specs=[pl.BlockSpec(memory_space=pltpu.VMEM)],
        out_specs=pl.BlockSpec(memory_space=pltpu.VMEM),
    )(gram_pair)


def staying_first(rotation, flag):
    half_width = rotation.shape[1] // 2
    swapped = jnp.concatenate([rotation[:, half_width:], rotation[:, :half_width]], axis=1)
    return jnp.where(flag == 1, swapped, rotation)


def basis_of(current, flag):
    gram_pair = butterfly_sum(contract(current, current), "row")
    rotation = orthogonal_iteration_kernel(gram_pair)
    if flag is not None:
        rotation = staying_first(rotation, flag)
    return gram_pair, rotation


def on_device(weight, move_flags):
    assert ROUNDS == 3
    half_width = weight.shape[1] // 2
    row_count = weight.shape[0] * lax.axis_size("row")
    cell_count = row_count * weight.shape[1] * lax.axis_size("pair")

    split = weight.shape[0] // 2
    previous_top = from_behind(weight[:split], "pair", 1)
    _, basis = basis_of(weight, move_flags[0, 0])
    basis_behind = from_behind(basis, "pair", 1)
    rotated_own = dot(weight, basis)
    moving_bottom = from_behind(rotated_own[split:, half_width:], "pair", 1)
    keep = weight.shape[0] * 7 // 8
    staying_bottom = from_behind(rotated_own[split:keep, :half_width], "pair", 1)
    rotated_top = dot(previous_top, basis_behind)
    arrived = jnp.concatenate([rotated_top[:, half_width:], moving_bottom], axis=0)
    current = jnp.concatenate([rotated_own[:, :half_width], arrived], axis=1)
    staying_behind = jnp.concatenate([rotated_top[:, :half_width], staying_bottom], axis=0)
    arrived_behind = from_behind(arrived[:keep], "pair", 1)

    gram_pair, basis = basis_of(current, move_flags[1, 0])
    basis_behind = from_behind(basis, "pair", 1)
    moving_part = basis[:, half_width:]
    arriving_gram = from_behind(contract(moving_part, dot(gram_pair, moving_part)), "pair", 1)
    rotated_own = dot(current, basis)
    moving_tail = from_behind(rotated_own[keep:, half_width:], "pair", 1)
    current_behind = jnp.concatenate([staying_behind, arrived_behind], axis=1)
    moving_head = dot(current_behind, basis_behind[:, half_width:])
    current = jnp.concatenate(
        [rotated_own[:, :half_width], jnp.concatenate([moving_head, moving_tail], axis=0)], axis=1
    )

    own_part = basis[:, :half_width]
    staying_gram = contract(own_part, dot(gram_pair, own_part))
    cross = butterfly_sum(contract(current[:, :half_width], current[:, half_width:]), "row")
    gram_pair = jnp.concatenate(
        [
            jnp.concatenate([staying_gram, cross], axis=1),
            jnp.concatenate([cross.T, arriving_gram], axis=1),
        ],
        axis=0,
    )
    rotation = orthogonal_iteration_kernel(gram_pair)
    rotated = dot(current, rotation)
    turned = jnp.sum(rotation * dot(gram_pair, rotation), axis=0)
    rotated = lax.optimization_barrier(rotated)
    squares_total = butterfly_sum(jnp.sum(turned), "pair")
    divisor = jnp.sqrt(squares_total / cell_count)
    columns = rotated / divisor
    norm_ratios = jnp.sqrt(turned / row_count) / divisor
    return (columns, norm_ratios)


def solution(mesh):
    return jax.shard_map(
        on_device,
        mesh=mesh,
        in_specs=(P("row", "pair"), P(None, "pair")),
        out_specs=(P("row", "pair"), P("pair")),
        check_vma=False,
    )
```

```python
import jax
import jax.numpy as jnp
from jax import lax
from jax.sharding import PartitionSpec as P
from jax.experimental import pallas as pl
from jax.experimental.pallas import tpu as pltpu

SWEEPS = 2
POLAR = 8
ROUNDS = 3


precise = lax.Precision.HIGH


def from_behind(block, axis, distance):
    devices = range(lax.axis_size(axis))
    route = [((i - distance) % len(devices), i) for i in devices]
    return lax.ppermute(block, axis, route)


def butterfly_sum(value, axis):
    size = lax.axis_size(axis)
    if size & (size - 1):
        return lax.psum(value, axis)
    step = 1
    while step < size:
        route = [(i, i ^ step) for i in range(size)]
        value = value + lax.ppermute(value, axis, route)
        step *= 2
    return value


def contract(left, right):
    return lax.dot_general(
        left, right, (((0,), (0,)), ((), ())), precision=precise, preferred_element_type=jnp.float32
    )


def dot(left, right):
    return jnp.dot(left, right, precision=precise, preferred_element_type=jnp.float32)


def orthogonal_iteration(gram_pair):
    rotation = jnp.eye(gram_pair.shape[0], dtype=jnp.float32)
    for sweep_index in range(SWEEPS):
        product = dot(gram_pair, rotation)
        normal = contract(product, product)
        scaled = product / jnp.sqrt(jnp.sqrt(jnp.sum(normal * normal)))
        for polar_index in range(POLAR):
            inner = contract(scaled, scaled)
            scaled = 1.5 * scaled - 0.5 * dot(scaled, inner)
        rotation = scaled
    return rotation


def split_bf16(value):
    high = value.astype(jnp.bfloat16)
    low = (value - high.astype(jnp.float32)).astype(jnp.bfloat16)
    return high, low


def dot_split(left, right):
    left_high, left_low = left
    right_high, right_low = right
    def one(a, b):
        return jnp.dot(a, b, preferred_element_type=jnp.float32)
    return one(left_high, right_high) + (one(left_high, right_low) + one(left_low, right_high))


def eigen_kernel(gram_ref, basis_ref):
    gram_pair = gram_ref[...]
    gram_parts = split_bf16(gram_pair)
    rotation = None
    for sweep_index in range(SWEEPS):
        product = gram_pair if rotation is None else dot_split(gram_parts, split_bf16(rotation))
        normal = dot_split(split_bf16(product.T), split_bf16(product))
        total = jnp.sum(jnp.sum(normal * normal, axis=1, keepdims=True), axis=0, keepdims=True)
        scaled = product / jnp.sqrt(jnp.sqrt(total))
        for polar_index in range(POLAR):
            parts = split_bf16(scaled)
            inner = dot_split(split_bf16(scaled.T), parts)
            scaled = 1.5 * scaled - 0.5 * dot_split(parts, split_bf16(inner))
        rotation = scaled
    basis_ref[...] = rotation


def orthogonal_iteration_kernel(gram_pair):
    return pl.pallas_call(
        eigen_kernel,
        out_shape=jax.ShapeDtypeStruct(gram_pair.shape, jnp.float32),
        in_specs=[pl.BlockSpec(memory_space=pltpu.VMEM)],
        out_specs=pl.BlockSpec(memory_space=pltpu.VMEM),
    )(gram_pair)


def staying_first(rotation, flag):
    half_width = rotation.shape[1] // 2
    swapped = jnp.concatenate([rotation[:, half_width:], rotation[:, :half_width]], axis=1)
    return jnp.where(flag == 1, swapped, rotation)


def basis_of(current, flag):
    gram_pair = butterfly_sum(contract(current, current), "row")
    rotation = orthogonal_iteration_kernel(gram_pair)
    if flag is not None:
        rotation = staying_first(rotation, flag)
    return gram_pair, rotation


def on_device(weight, move_flags):
    assert ROUNDS == 3
    half_width = weight.shape[1] // 2
    row_count = weight.shape[0] * lax.axis_size("row")
    cell_count = row_count * weight.shape[1] * lax.axis_size("pair")

    split = weight.shape[0] // 2
    previous_top = from_behind(weight[:split], "pair", 1)
    _, basis = basis_of(weight, move_flags[0, 0])
    basis_behind = from_behind(basis, "pair", 1)
    rotated_own = dot(weight, basis)
    moving_bottom = from_behind(rotated_own[split:, half_width:], "pair", 1)
    keep = weight.shape[0] * 15 // 16
    staying_bottom = from_behind(rotated_own[split:keep, :half_width], "pair", 1)
    rotated_top = dot(previous_top, basis_behind)
    arrived = jnp.concatenate([rotated_top[:, half_width:], moving_bottom], axis=0)
    current = jnp.concatenate([rotated_own[:, :half_width], arrived], axis=1)
    staying_behind = jnp.concatenate([rotated_top[:, :half_width], staying_bottom], axis=0)
    arrived_behind = from_behind(arrived[:keep], "pair", 1)

    gram_pair, basis = basis_of(current, move_flags[1, 0])
    basis_behind = from_behind(basis, "pair", 1)
    moving_part = basis[:, half_width:]
    arriving_gram = from_behind(contract(moving_part, dot(gram_pair, moving_part)), "pair", 1)
    rotated_own = dot(current, basis)
    moving_tail = from_behind(rotated_own[keep:, half_width:], "pair", 1)
    current_behind = jnp.concatenate([staying_behind, arrived_behind], axis=1)
    moving_head = dot(current_behind, basis_behind[:, half_width:])
    current = jnp.concatenate(
        [rotated_own[:, :half_width], jnp.concatenate([moving_head, moving_tail], axis=0)], axis=1
    )

    own_part = basis[:, :half_width]
    staying_gram = contract(own_part, dot(gram_pair, own_part))
    cross = butterfly_sum(contract(current[:, :half_width], current[:, half_width:]), "row")
    gram_pair = jnp.concatenate(
        [
            jnp.concatenate([staying_gram, cross], axis=1),
            jnp.concatenate([cross.T, arriving_gram], axis=1),
        ],
        axis=0,
    )
    rotation = orthogonal_iteration_kernel(gram_pair)
    rotated = dot(current, rotation)
    turned = jnp.sum(rotation * dot(gram_pair, rotation), axis=0)
    rotated = lax.optimization_barrier(rotated)
    squares_total = butterfly_sum(jnp.sum(turned), "pair")
    divisor = jnp.sqrt(squares_total / cell_count)
    columns = rotated / divisor
    norm_ratios = jnp.sqrt(turned / row_count) / divisor
    return (columns, norm_ratios)


def solution(mesh):
    return jax.shard_map(
        on_device,
        mesh=mesh,
        in_specs=(P("row", "pair"), P(None, "pair")),
        out_specs=(P("row", "pair"), P("pair")),
        check_vma=False,
    )
```

```python
import jax
import jax.numpy as jnp
from jax import lax
from jax.sharding import PartitionSpec as P
from jax.experimental import pallas as pl
from jax.experimental.pallas import tpu as pltpu

SWEEPS = 2
POLAR = 8
ROUNDS = 3


precise = lax.Precision.HIGH


def from_behind(block, axis, distance):
    devices = range(lax.axis_size(axis))
    route = [((i - distance) % len(devices), i) for i in devices]
    return lax.ppermute(block, axis, route)


def butterfly_sum(value, axis):
    size = lax.axis_size(axis)
    if size & (size - 1):
        return lax.psum(value, axis)
    step = 1
    while step < size:
        route = [(i, i ^ step) for i in range(size)]
        value = value + lax.ppermute(value, axis, route)
        step *= 2
    return value


def contract(left, right):
    return lax.dot_general(
        left, right, (((0,), (0,)), ((), ())), precision=precise, preferred_element_type=jnp.float32
    )


def dot(left, right):
    return jnp.dot(left, right, precision=precise, preferred_element_type=jnp.float32)


def orthogonal_iteration(gram_pair):
    rotation = jnp.eye(gram_pair.shape[0], dtype=jnp.float32)
    for sweep_index in range(SWEEPS):
        product = dot(gram_pair, rotation)
        normal = contract(product, product)
        scaled = product / jnp.sqrt(jnp.sqrt(jnp.sum(normal * normal)))
        for polar_index in range(POLAR):
            inner = contract(scaled, scaled)
            scaled = 1.5 * scaled - 0.5 * dot(scaled, inner)
        rotation = scaled
    return rotation


def split_bf16(value):
    high = value.astype(jnp.bfloat16)
    low = (value - high.astype(jnp.float32)).astype(jnp.bfloat16)
    return high, low


def dot_split(left, right):
    left_high, left_low = left
    right_high, right_low = right
    def one(a, b):
        return jnp.dot(a, b, preferred_element_type=jnp.float32)
    return one(left_high, right_high) + (one(left_high, right_low) + one(left_low, right_high))


def eigen_kernel(gram_ref, basis_ref):
    gram_pair = gram_ref[...]
    gram_parts = split_bf16(gram_pair)
    rotation = None
    for sweep_index in range(SWEEPS):
        product = gram_pair if rotation is None else dot_split(gram_parts, split_bf16(rotation))
        normal = dot_split(split_bf16(product.T), split_bf16(product))
        total = jnp.sum(jnp.sum(normal * normal, axis=1, keepdims=True), axis=0, keepdims=True)
        scaled = product / jnp.sqrt(jnp.sqrt(total))
        for polar_index in range(POLAR):
            parts = split_bf16(scaled)
            inner = dot_split(split_bf16(scaled.T), parts)
            scaled = 1.5 * scaled - 0.5 * dot_split(parts, split_bf16(inner))
        rotation = scaled
    basis_ref[...] = rotation


def orthogonal_iteration_kernel(gram_pair):
    return pl.pallas_call(
        eigen_kernel,
        out_shape=jax.ShapeDtypeStruct(gram_pair.shape, jnp.float32),
        in_specs=[pl.BlockSpec(memory_space=pltpu.VMEM)],
        out_specs=pl.BlockSpec(memory_space=pltpu.VMEM),
    )(gram_pair)


def staying_first(rotation, flag):
    half_width = rotation.shape[1] // 2
    swapped = jnp.concatenate([rotation[:, half_width:], rotation[:, :half_width]], axis=1)
    return jnp.where(flag == 1, swapped, rotation)


def basis_of(current, flag):
    gram_pair = butterfly_sum(contract(current, current), "row")
    rotation = orthogonal_iteration_kernel(gram_pair)
    if flag is not None:
        rotation = staying_first(rotation, flag)
    return gram_pair, rotation


def on_device(weight, move_flags):
    assert ROUNDS == 3
    half_width = weight.shape[1] // 2
    row_count = weight.shape[0] * lax.axis_size("row")
    cell_count = row_count * weight.shape[1] * lax.axis_size("pair")

    split = weight.shape[0] * 9 // 16
    previous_top = from_behind(weight[:split], "pair", 1)
    _, basis = basis_of(weight, move_flags[0, 0])
    basis_behind = from_behind(basis, "pair", 1)
    rotated_own = dot(weight, basis)
    moving_bottom = from_behind(rotated_own[split:, half_width:], "pair", 1)
    keep = weight.shape[0] * 7 // 8
    staying_bottom = from_behind(rotated_own[split:keep, :half_width], "pair", 1)
    rotated_top = dot(previous_top, basis_behind)
    arrived = jnp.concatenate([rotated_top[:, half_width:], moving_bottom], axis=0)
    current = jnp.concatenate([rotated_own[:, :half_width], arrived], axis=1)
    staying_behind = jnp.concatenate([rotated_top[:, :half_width], staying_bottom], axis=0)
    arrived_behind = from_behind(arrived[:keep], "pair", 1)

    gram_pair, basis = basis_of(current, move_flags[1, 0])
    basis_behind = from_behind(basis, "pair", 1)
    moving_part = basis[:, half_width:]
    arriving_gram = from_behind(contract(moving_part, dot(gram_pair, moving_part)), "pair", 1)
    rotated_own = dot(current, basis)
    moving_tail = from_behind(rotated_own[keep:, half_width:], "pair", 1)
    current_behind = jnp.concatenate([staying_behind, arrived_behind], axis=1)
    moving_head = dot(current_behind, basis_behind[:, half_width:])
    current = jnp.concatenate(
        [rotated_own[:, :half_width], jnp.concatenate([moving_head, moving_tail], axis=0)], axis=1
    )

    own_part = basis[:, :half_width]
    staying_gram = contract(own_part, dot(gram_pair, own_part))
    cross = butterfly_sum(contract(current[:, :half_width], current[:, half_width:]), "row")
    gram_pair = jnp.concatenate(
        [
            jnp.concatenate([staying_gram, cross], axis=1),
            jnp.concatenate([cross.T, arriving_gram], axis=1),
        ],
        axis=0,
    )
    rotation = orthogonal_iteration_kernel(gram_pair)
    rotated = dot(current, rotation)
    turned = jnp.sum(rotation * dot(gram_pair, rotation), axis=0)
    rotated = lax.optimization_barrier(rotated)
    squares_total = butterfly_sum(jnp.sum(turned), "pair")
    divisor = jnp.sqrt(squares_total / cell_count)
    columns = rotated / divisor
    norm_ratios = jnp.sqrt(turned / row_count) / divisor
    return (columns, norm_ratios)


def solution(mesh):
    return jax.shard_map(
        on_device,
        mesh=mesh,
        in_specs=(P("row", "pair"), P(None, "pair")),
        out_specs=(P("row", "pair"), P("pair")),
        check_vma=False,
    )
```

```python
import jax
import jax.numpy as jnp
from jax import lax
from jax.sharding import PartitionSpec as P
from jax.experimental import pallas as pl
from jax.experimental.pallas import tpu as pltpu

SWEEPS = 2
POLAR = 8
ROUNDS = 3


precise = lax.Precision.HIGH


def from_behind(block, axis, distance):
    devices = range(lax.axis_size(axis))
    route = [((i - distance) % len(devices), i) for i in devices]
    return lax.ppermute(block, axis, route)


def butterfly_sum(value, axis):
    size = lax.axis_size(axis)
    if size & (size - 1):
        return lax.psum(value, axis)
    step = 1
    while step < size:
        route = [(i, i ^ step) for i in range(size)]
        value = value + lax.ppermute(value, axis, route)
        step *= 2
    return value


def contract(left, right):
    return lax.dot_general(
        left, right, (((0,), (0,)), ((), ())), precision=precise, preferred_element_type=jnp.float32
    )


def dot(left, right):
    return jnp.dot(left, right, precision=precise, preferred_element_type=jnp.float32)


def orthogonal_iteration(gram_pair):
    rotation = jnp.eye(gram_pair.shape[0], dtype=jnp.float32)
    for sweep_index in range(SWEEPS):
        product = dot(gram_pair, rotation)
        normal = contract(product, product)
        scaled = product / jnp.sqrt(jnp.sqrt(jnp.sum(normal * normal)))
        for polar_index in range(POLAR):
            inner = contract(scaled, scaled)
            scaled = 1.5 * scaled - 0.5 * dot(scaled, inner)
        rotation = scaled
    return rotation


def split_bf16(value):
    high = value.astype(jnp.bfloat16)
    low = (value - high.astype(jnp.float32)).astype(jnp.bfloat16)
    return high, low


def dot_split(left, right):
    left_high, left_low = left
    right_high, right_low = right
    def one(a, b):
        return jnp.dot(a, b, preferred_element_type=jnp.float32)
    return one(left_high, right_high) + (one(left_high, right_low) + one(left_low, right_high))


def eigen_kernel(gram_ref, basis_ref):
    gram_pair = gram_ref[...]
    gram_parts = split_bf16(gram_pair)
    rotation = None
    for sweep_index in range(SWEEPS):
        product = gram_pair if rotation is None else dot_split(gram_parts, split_bf16(rotation))
        normal = dot_split(split_bf16(product.T), split_bf16(product))
        total = jnp.sum(jnp.sum(normal * normal, axis=1, keepdims=True), axis=0, keepdims=True)
        scaled = product / jnp.sqrt(jnp.sqrt(total))
        for polar_index in range(POLAR):
            parts = split_bf16(scaled)
            inner = dot_split(split_bf16(scaled.T), parts)
            scaled = 1.5 * scaled - 0.5 * dot_split(parts, split_bf16(inner))
        rotation = scaled
    basis_ref[...] = rotation


def orthogonal_iteration_kernel(gram_pair):
    return pl.pallas_call(
        eigen_kernel,
        out_shape=jax.ShapeDtypeStruct(gram_pair.shape, jnp.float32),
        in_specs=[pl.BlockSpec(memory_space=pltpu.VMEM)],
        out_specs=pl.BlockSpec(memory_space=pltpu.VMEM),
    )(gram_pair)


def staying_first(rotation, flag):
    half_width = rotation.shape[1] // 2
    swapped = jnp.concatenate([rotation[:, half_width:], rotation[:, :half_width]], axis=1)
    return jnp.where(flag == 1, swapped, rotation)


def basis_of(current, flag):
    gram_pair = butterfly_sum(contract(current, current), "row")
    rotation = orthogonal_iteration_kernel(gram_pair)
    if flag is not None:
        rotation = staying_first(rotation, flag)
    return gram_pair, rotation


def on_device(weight, move_flags):
    assert ROUNDS == 3
    half_width = weight.shape[1] // 2
    row_count = weight.shape[0] * lax.axis_size("row")
    cell_count = row_count * weight.shape[1] * lax.axis_size("pair")

    split = weight.shape[0] * 7 // 16
    previous_top = from_behind(weight[:split], "pair", 1)
    _, basis = basis_of(weight, move_flags[0, 0])
    basis_behind = from_behind(basis, "pair", 1)
    rotated_own = dot(weight, basis)
    moving_bottom = from_behind(rotated_own[split:, half_width:], "pair", 1)
    keep = weight.shape[0] * 7 // 8
    staying_bottom = from_behind(rotated_own[split:keep, :half_width], "pair", 1)
    rotated_top = dot(previous_top, basis_behind)
    arrived = jnp.concatenate([rotated_top[:, half_width:], moving_bottom], axis=0)
    current = jnp.concatenate([rotated_own[:, :half_width], arrived], axis=1)
    staying_behind = jnp.concatenate([rotated_top[:, :half_width], staying_bottom], axis=0)
    arrived_behind = from_behind(arrived[:keep], "pair", 1)

    gram_pair, basis = basis_of(current, move_flags[1, 0])
    basis_behind = from_behind(basis, "pair", 1)
    moving_part = basis[:, half_width:]
    arriving_gram = from_behind(contract(moving_part, dot(gram_pair, moving_part)), "pair", 1)
    rotated_own = dot(current, basis)
    moving_tail = from_behind(rotated_own[keep:, half_width:], "pair", 1)
    current_behind = jnp.concatenate([staying_behind, arrived_behind], axis=1)
    moving_head = dot(current_behind, basis_behind[:, half_width:])
    current = jnp.concatenate(
        [rotated_own[:, :half_width], jnp.concatenate([moving_head, moving_tail], axis=0)], axis=1
    )

    own_part = basis[:, :half_width]
    staying_gram = contract(own_part, dot(gram_pair, own_part))
    cross = butterfly_sum(contract(current[:, :half_width], current[:, half_width:]), "row")
    gram_pair = jnp.concatenate(
        [
            jnp.concatenate([staying_gram, cross], axis=1),
            jnp.concatenate([cross.T, arriving_gram], axis=1),
        ],
        axis=0,
    )
    rotation = orthogonal_iteration_kernel(gram_pair)
    rotated = dot(current, rotation)
    turned = jnp.sum(rotation * dot(gram_pair, rotation), axis=0)
    rotated = lax.optimization_barrier(rotated)
    squares_total = butterfly_sum(jnp.sum(turned), "pair")
    divisor = jnp.sqrt(squares_total / cell_count)
    columns = rotated / divisor
    norm_ratios = jnp.sqrt(turned / row_count) / divisor
    return (columns, norm_ratios)


def solution(mesh):
    return jax.shard_map(
        on_device,
        mesh=mesh,
        in_specs=(P("row", "pair"), P(None, "pair")),
        out_specs=(P("row", "pair"), P("pair")),
        check_vma=False,
    )
```
